128 devices in a mesh: az: 16 (over x_hi, z, core), tm: 8 (over x_lo, y).
Axes of the slice: x: 4 (x_hi: 2, x_lo: 2; x = x_hi * 2 + x_lo), y: 4, z: 4, core: 2. Of those that a mesh axis runs over, the one named last changes fastest.
Arguments:
- pressure: bfloat16 [16, 64, 128, 4096], P(None, 'az', 'tm'), may hold values from -6 to 6
- offsets: int32 [128, 16], P('tm'), may hold values from -1 to 0
- frac: float32 [128, 16], P('tm'), may hold values from 0 to 1
Outputs:
- csm: float32 [256, 2, 1024, 1024], P('tm', None, 'az')
The draws below stay inside these ranges and needn't reach their ends.
All inputs are finite; a program needn't handle non-finite values.
Results may differ from the reference program's by a relative error of at most 0.0065.
Values may be sent and summed in bfloat16 or wider, within the bound.
No kernel may reach another device: no remote copies, remote signals or barrier semaphores. Data moves between devices by JAX's collectives and lax.ppermute only.
A program may use at most 192 MiB of HBM per device.

```python
import math
import jax
import jax.numpy as jnp
from jax import lax

CYCLES = 16
CYCLE_MICS = 64
BLOCK_LEN = 4096
FREQS = 256
SUBS = 16
BLOCKS = 128


def plant(result, key, smallest, top_value):
    extent = result.shape
    place = [jax.random.randint(jax.random.fold_in(key, axis), (), 0, extent[axis]) for axis in range(len(extent))]
    result = result.at[tuple(place)].set(smallest)
    longest = extent.index(max(extent))
    place[longest] = (place[longest] + 1) % extent[longest]
    return result.at[tuple(place)].set(top_value)


def block_scale(key, shape, cuts, smallest, largest):
    loudness, own = 1.0, jax.random.fold_in(key, 6)
    for axis_at, blocks in cuts:
        draws = jnp.exp(jax.random.uniform(jax.random.fold_in(own, axis_at), (blocks,), jnp.float32, smallest / len(cuts), largest / len(cuts)))
        loudness = loudness * jnp.repeat(draws, shape[axis_at] // blocks).reshape([-1 if axis == axis_at else 1 for axis in range(len(shape))])
    return loudness


def normal_values(stream_key, shape, deviation, most, cuts=(), kind=jnp.bfloat16):
    values = jax.random.normal(stream_key, shape, jnp.float32) * deviation
    if len(cuts) > 0:
        values = block_scale(stream_key, shape, cuts, -0.22, 0.18) * values
    return jnp.clip(values, min=-most, max=most).astype(kind)


def setup_inputs(seed: int = 0) -> dict:
    key_list = jax.random.split(jax.random.key(seed), 4)
    pressure = normal_values(key_list[0], (CYCLES, CYCLE_MICS, BLOCKS, BLOCK_LEN), 1.0, 6.0, ((1, 16), (2, 8)))
    offsets = plant(jax.random.randint(key_list[1], (BLOCKS, SUBS), -1, 1), jax.random.fold_in(key_list[1], 1), -1, 0).astype(jnp.int32)
    frac = jnp.clip(1.0 * jax.random.uniform(key_list[2], (BLOCKS, SUBS), jnp.float32) ** block_scale(key_list[2], (BLOCKS, SUBS), ((0, 8),), -0.2, 0.2), 0.0, 1.0)
    return dict(pressure=pressure, offsets=offsets, frac=frac)


def dft_table(length, freqs):
    times = jnp.arange(length, dtype=jnp.int32)
    bins = jnp.arange(1, freqs + 1, dtype=jnp.int32)
    phase = (times[:, None] * bins[None, :] % length).astype(jnp.float32) * (2.0 * math.pi / length)
    hann = 0.5 - 0.5 * jnp.cos(times.astype(jnp.float32) * (2.0 * math.pi / length))
    factor = hann[:, None] / math.sqrt(3.0 * length / 8.0)
    return jnp.concatenate([factor * jnp.cos(phase), -factor * jnp.sin(phase)], axis=1).astype(jnp.bfloat16)

def interp_weights(offsets, frac):
    rows = []
    for shift in range(-1, 2):
        low = (offsets == shift).astype(frac.dtype)
        high = (offsets + 1 == shift).astype(frac.dtype)
        rows.append((1.0 - frac) * low + frac * high)
    return jnp.stack(rows, 0)

def reference(pressure, offsets, frac):
    table = dft_table(BLOCK_LEN, FREQS)
    weights = interp_weights(offsets, frac)
    sub_len = BLOCK_LEN // SUBS

    def one_block(index):
        block = lax.dynamic_index_in_dim(pressure, index, 2, keepdims=False)
        coef = lax.dynamic_index_in_dim(weights, index, 1, keepdims=False)
        total = jnp.zeros((CYCLES, CYCLE_MICS, SUBS, sub_len), jnp.float32)
        for shift in range(-1, 2):
            moved = jnp.roll(block, -shift, axis=1).reshape(CYCLES, CYCLE_MICS, SUBS, sub_len)
            total = total + coef[shift + 1][None, None, :, None] * moved.astype(jnp.float32)
        virtual = total.astype(jnp.bfloat16).reshape(CYCLES * CYCLE_MICS, BLOCK_LEN)
        spec = jnp.dot(virtual, table, preferred_element_type=jnp.float32).astype(jnp.bfloat16)
        return spec.reshape(CYCLES, CYCLE_MICS, 2, FREQS)
    spectra = lax.map(one_block, jnp.arange(BLOCKS, dtype=jnp.int32))
    stacked = spectra.transpose(4, 2, 1, 0, 3).reshape(FREQS, CYCLE_MICS * CYCLES, BLOCKS * 2)

    def one_freq(rows):
        rows32 = rows.astype(jnp.float32)
        split = rows32.reshape(CYCLE_MICS * CYCLES, BLOCKS, 2)
        turned = jnp.stack([split[:, :, 1], -split[:, :, 0]], -1).reshape(CYCLE_MICS * CYCLES, BLOCKS * 2)
        real = jnp.dot(rows32, rows32.T)
        imag = jnp.dot(turned, rows32.T)
        return jnp.stack([real, imag], 0) * (1.0 / BLOCKS)
    return lax.map(one_freq, stacked)
```

```python
import math

import jax
import jax.numpy as jnp
from jax import lax
from jax.sharding import PartitionSpec as P

FREQS = 256


def dft_table(length, freqs):
    times = jnp.arange(length, dtype=jnp.int32)
    bins = jnp.arange(1, freqs + 1, dtype=jnp.int32)
    phase = (times[:, None] * bins[None, :] % length).astype(jnp.float32) * (2.0 * math.pi / length)
    hann = 0.5 - 0.5 * jnp.cos(times.astype(jnp.float32) * (2.0 * math.pi / length))
    factor = hann[:, None] / math.sqrt(3.0 * length / 8.0)
    return jnp.concatenate([factor * jnp.cos(phase), -factor * jnp.sin(phase)], axis=1).astype(
        jnp.bfloat16
    )


def interp_weights(offsets, frac):
    rows = []
    for shift in range(-1, 2):
        low = (offsets == shift).astype(frac.dtype)
        high = (offsets + 1 == shift).astype(frac.dtype)
        rows.append((1.0 - frac) * low + frac * high)
    return jnp.stack(rows, 0)


def shards(pressure, offsets, frac):
    cycles, sector, blocks, length = pressure.shape
    subs = offsets.shape[1]
    sub_len = length // subs
    n_az = lax.axis_size("az")
    n_tm = lax.axis_size("tm")
    forward = [(i, (i + 1) % n_az) for i in range(n_az)]
    backward = [((i + 1) % n_az, i) for i in range(n_az)]
    left = lax.ppermute(pressure[:, sector - 1 :], "az", forward)
    right = lax.ppermute(pressure[:, :1], "az", backward)
    weights = jnp.repeat(interp_weights(offsets, frac), sub_len, axis=2)[:, None, None]
    prev = jnp.concatenate([left, pressure[:, :-1]], axis=1).astype(jnp.float32)
    nxt = jnp.concatenate([pressure[:, 1:], right], axis=1).astype(jnp.float32)
    total = weights[0] * prev + weights[1] * pressure.astype(jnp.float32) + weights[2] * nxt
    virtual = total.astype(jnp.bfloat16).reshape(cycles * sector * blocks, length)
    table = dft_table(length, FREQS)
    freqs = FREQS
    spectra = jnp.dot(virtual, table, preferred_element_type=jnp.float32).astype(jnp.bfloat16)
    spectra = spectra.reshape(cycles, sector, blocks, 2, freqs).transpose(4, 1, 0, 3, 2)
    local_rows = sector * cycles
    spectra = spectra.reshape(n_tm, freqs // n_tm, local_rows, 2, blocks)
    shared = lax.all_to_all(spectra, "tm", 0, 0, tiled=True)
    shared = shared.reshape(n_tm, freqs // n_tm, local_rows, 2, blocks).transpose(1, 2, 3, 0, 4)
    fl = freqs // n_tm
    shared = shared.reshape(fl, local_rows, 2, n_tm * blocks)
    rows = shared.reshape(fl, local_rows, 2 * n_tm * blocks)
    turned = jnp.concatenate([shared[:, :, 1], -shared[:, :, 0]], axis=2)
    lhs = jnp.stack([rows, turned], 1)
    columns = lax.all_gather(rows, "az", axis=1, tiled=True)
    result = jnp.einsum("fcqk,fpk->fcqp", lhs, columns, preferred_element_type=jnp.float32)
    return result * (1.0 / (n_tm * blocks))


def solution(mesh):
    return jax.shard_map(
        shards,
        mesh=mesh,
        in_specs=(P(None, "az", "tm", None), P("tm", None), P("tm", None)),
        out_specs=P("tm", None, "az", None),
        check_vma=False,
    )
```

```python
import math

import jax
import jax.numpy as jnp
from jax import lax
from jax.sharding import Mesh
from jax.sharding import PartitionSpec as P

FREQS = 256
CHUNKS = 4
AZ = ("xh", "z", "core")
TM = ("xl", "y")
CHIPS = ("xh", "z")


def dft_table(length, freqs):
    step = 64
    bins = jnp.arange(1, freqs + 1, dtype=jnp.int32)
    high = jnp.arange(length // step, dtype=jnp.int32)
    low = jnp.arange(step, dtype=jnp.int32)
    scale = 2.0 * math.pi / length
    a = (high[:, None] * step * bins[None, :] % length).astype(jnp.float32) * scale
    b = (low[:, None] * bins[None, :] % length).astype(jnp.float32) * scale
    ca, sa = jnp.cos(a)[:, None], jnp.sin(a)[:, None]
    cb, sb = jnp.cos(b)[None], jnp.sin(b)[None]
    ca, sa, cb, sb = lax.optimization_barrier((ca, sa, cb, sb))
    cos = (ca * cb - sa * sb).reshape(length, freqs)
    sin = (sa * cb + ca * sb).reshape(length, freqs)
    times = jnp.arange(length, dtype=jnp.int32)
    hann = 0.5 - 0.5 * jnp.cos(times.astype(jnp.float32) * scale)
    factor = hann[:, None] / math.sqrt(3.0 * length / 8.0)
    return jnp.concatenate([factor * cos, -factor * sin], axis=1).astype(jnp.bfloat16)


def interp_weights(offsets, frac):
    rows = []
    for shift in range(-1, 2):
        low = (offsets == shift).astype(frac.dtype)
        high = (offsets + 1 == shift).astype(frac.dtype)
        rows.append((1.0 - frac) * low + frac * high)
    return jnp.stack(rows, 0)


def shards(pressure, offsets, frac):
    cycles, sector, blocks, length = pressure.shape
    subs = offsets.shape[1]
    sub_len = length // subs
    n_az = lax.axis_size(AZ)
    n_tm = lax.axis_size(TM)
    forward = [(i, (i + 1) % n_az) for i in range(n_az)]
    backward = [((i + 1) % n_az, i) for i in range(n_az)]
    left = lax.ppermute(pressure[:, sector - 1 :], AZ, forward)
    right = lax.ppermute(pressure[:, :1], AZ, backward)
    weights = jnp.repeat(interp_weights(offsets, frac), sub_len, axis=2)[:, None, None]
    prev = jnp.concatenate([left, pressure[:, :-1]], axis=1).astype(jnp.float32)
    nxt = jnp.concatenate([pressure[:, 1:], right], axis=1).astype(jnp.float32)
    total = weights[0] * prev + weights[1] * pressure.astype(jnp.float32) + weights[2] * nxt
    virtual = total.astype(jnp.bfloat16).reshape(cycles * sector * blocks, length)
    table = dft_table(length, FREQS)
    fl = FREQS // n_tm
    spectra = lax.dot_general(
        table, virtual, (((0,), (1,)), ((), ())), preferred_element_type=jnp.float32
    ).astype(jnp.bfloat16)
    spectra = spectra.reshape(2, n_tm, fl, cycles, sector, blocks).transpose(1, 2, 0, 3, 4, 5)
    shared = lax.all_to_all(spectra, TM, 0, 0, tiled=True)
    local_rows = sector * cycles
    width = n_tm * blocks
    x = shared.transpose(1, 4, 3, 2, 0, 5).reshape(fl, local_rows, 2, width)
    rows = x.reshape(fl, local_rows, 2 * width)
    turned = jnp.concatenate([x[:, :, 1], -x[:, :, 0]], axis=2)
    lhs = jnp.stack([rows, turned], 1).reshape(fl, 2, local_rows, 2, width)
    core = lax.axis_index("core")
    chip = lax.all_gather(x, "core", axis=1, tiled=True)
    mine = lax.dynamic_index_in_dim(chip, core, axis=2, keepdims=False)
    l_own = lax.dynamic_index_in_dim(lhs, core, axis=3, keepdims=False)
    l_other = lax.dynamic_index_in_dim(lhs, 1 - core, axis=3, keepdims=False)
    fc = fl // CHUNKS
    outs = []
    for j in range(CHUNKS):
        part = mine[j * fc : (j + 1) * fc]
        own_cols = lax.all_gather(part, CHIPS, axis=1, tiled=True)
        other_cols = lax.ppermute(own_cols, "core", [(0, 1), (1, 0)])
        res = jnp.einsum(
            "fcqk,fpk->fcqp", l_own[j * fc : (j + 1) * fc], own_cols,
            preferred_element_type=jnp.float32,
        ) + jnp.einsum(
            "fcqk,fpk->fcqp", l_other[j * fc : (j + 1) * fc], other_cols,
            preferred_element_type=jnp.float32,
        )
        outs.append(res * (1.0 / width))
    return jnp.concatenate(outs, 0)


def solution(mesh):
    az, tm = mesh.devices.shape
    fine = Mesh(mesh.devices.reshape(2, az // 4, 2, 2, tm // 2), ("xh", "z", "core", "xl", "y"))
    return jax.shard_map(
        shards,
        mesh=fine,
        in_specs=(P(None, AZ, TM, None), P(TM, None), P(TM, None)),
        out_specs=P(TM, None, AZ, None),
        check_vma=False,
    )
```

```python
import math

import jax
import jax.numpy as jnp
from jax import lax
from jax.sharding import PartitionSpec as P

FREQS = 256


def dft_table(length, freqs):
    step = 64
    bins = jnp.arange(1, freqs + 1, dtype=jnp.int32)
    high = jnp.arange(length // step, dtype=jnp.int32)
    low = jnp.arange(step, dtype=jnp.int32)
    scale = 2.0 * math.pi / length
    a = (high[:, None] * step * bins[None, :] % length).astype(jnp.float32) * scale
    b = (low[:, None] * bins[None, :] % length).astype(jnp.float32) * scale
    ca, sa = jnp.cos(a)[:, None], jnp.sin(a)[:, None]
    cb, sb = jnp.cos(b)[None], jnp.sin(b)[None]
    ca, sa, cb, sb = lax.optimization_barrier((ca, sa, cb, sb))
    cos = (ca * cb - sa * sb).reshape(length, freqs)
    sin = (sa * cb + ca * sb).reshape(length, freqs)
    times = jnp.arange(length, dtype=jnp.int32)
    hann = 0.5 - 0.5 * jnp.cos(times.astype(jnp.float32) * scale)
    factor = hann[:, None] / math.sqrt(3.0 * length / 8.0)
    return jnp.concatenate([factor * cos, -factor * sin], axis=1).astype(jnp.bfloat16)


def interp_weights(offsets, frac):
    rows = []
    for shift in range(-1, 2):
        low = (offsets == shift).astype(frac.dtype)
        high = (offsets + 1 == shift).astype(frac.dtype)
        rows.append((1.0 - frac) * low + frac * high)
    return jnp.stack(rows, 0)


def shards(pressure, offsets, frac):
    cycles, sector, blocks, length = pressure.shape
    subs = offsets.shape[1]
    sub_len = length // subs
    n_az = lax.axis_size("az")
    n_tm = lax.axis_size("tm")
    forward = [(i, (i + 1) % n_az) for i in range(n_az)]
    backward = [((i + 1) % n_az, i) for i in range(n_az)]
    left = lax.ppermute(pressure[:, sector - 1 :], "az", forward)
    right = lax.ppermute(pressure[:, :1], "az", backward)
    weights = jnp.repeat(interp_weights(offsets, frac), sub_len, axis=2)[:, None, None]
    prev = jnp.concatenate([left, pressure[:, :-1]], axis=1).astype(jnp.float32)
    nxt = jnp.concatenate([pressure[:, 1:], right], axis=1).astype(jnp.float32)
    total = weights[0] * prev + weights[1] * pressure.astype(jnp.float32) + weights[2] * nxt
    virtual = total.astype(jnp.bfloat16).transpose(2, 1, 0, 3).reshape(blocks * sector * cycles, length)
    table = dft_table(length, FREQS)
    fl = FREQS // n_tm
    local_rows = sector * cycles
    width = n_tm * blocks
    spectra = lax.dot_general(
        table, virtual, (((0,), (1,)), ((), ())), preferred_element_type=jnp.float32
    ).astype(jnp.bfloat16)
    spectra = spectra.reshape(2, n_tm, fl, blocks * local_rows).transpose(1, 0, 2, 3)
    shared = lax.all_to_all(spectra, "tm", 0, 0, tiled=True)
    shared = shared.reshape(n_tm, 2, fl, blocks, local_rows)
    x = shared.transpose(2, 4, 0, 1, 3)
    rows = x.reshape(fl, local_rows, 2 * width)
    turned = jnp.stack([x[:, :, :, 1], -x[:, :, :, 0]], 3).reshape(fl, local_rows, 2 * width)
    lhs = jnp.stack([rows, turned], 1)
    columns = lax.all_gather(rows, "az", axis=1, tiled=True)
    result = jnp.einsum("fcqk,fpk->fcqp", lhs, columns, preferred_element_type=jnp.float32)
    return result * (1.0 / width)


def solution(mesh):
    return jax.shard_map(
        shards,
        mesh=mesh,
        in_specs=(P(None, "az", "tm", None), P("tm", None), P("tm", None)),
        out_specs=P("tm", None, "az", None),
        check_vma=False,
    )
```

```python
import math

import jax
import jax.numpy as jnp
from jax import lax
from jax.sharding import PartitionSpec as P

FREQS = 256
BLOCK_CHUNKS = 2


def dft_table(length, freqs):
    step = 64
    bins = jnp.arange(1, freqs + 1, dtype=jnp.int32)
    high = jnp.arange(length // step, dtype=jnp.int32)
    low = jnp.arange(step, dtype=jnp.int32)
    scale = 2.0 * math.pi / length
    a = (high[:, None] * step * bins[None, :] % length).astype(jnp.float32) * scale
    b = (low[:, None] * bins[None, :] % length).astype(jnp.float32) * scale
    ca, sa = jnp.cos(a)[:, None], jnp.sin(a)[:, None]
    cb, sb = jnp.cos(b)[None], jnp.sin(b)[None]
    ca, sa, cb, sb = lax.optimization_barrier((ca, sa, cb, sb))
    cos = (ca * cb - sa * sb).reshape(length, freqs)
    sin = (sa * cb + ca * sb).reshape(length, freqs)
    times = jnp.arange(length, dtype=jnp.int32)
    hann = 0.5 - 0.5 * jnp.cos(times.astype(jnp.float32) * scale)
    factor = hann[:, None] / math.sqrt(3.0 * length / 8.0)
    return jnp.concatenate([factor * cos, -factor * sin], axis=1).astype(jnp.bfloat16)


def interp_weights(offsets, frac):
    rows = []
    for shift in range(-1, 2):
        low = (offsets == shift).astype(frac.dtype)
        high = (offsets + 1 == shift).astype(frac.dtype)
        rows.append((1.0 - frac) * low + frac * high)
    return jnp.stack(rows, 0)


def shards(pressure, offsets, frac):
    cycles, sector, blocks, length = pressure.shape
    subs = offsets.shape[1]
    sub_len = length // subs
    n_az = lax.axis_size("az")
    n_tm = lax.axis_size("tm")
    forward = [(i, (i + 1) % n_az) for i in range(n_az)]
    backward = [((i + 1) % n_az, i) for i in range(n_az)]
    table = dft_table(length, FREQS)
    all_weights = jnp.repeat(interp_weights(offsets, frac), sub_len, axis=2)[:, None, None]
    fl = FREQS // n_tm
    local_rows = sector * cycles
    nb = blocks // BLOCK_CHUNKS
    result = None
    for j in range(BLOCK_CHUNKS):
        block = pressure[:, :, j * nb : (j + 1) * nb]
        left = lax.ppermute(block[:, sector - 1 :], "az", forward)
        right = lax.ppermute(block[:, :1], "az", backward)
        weights = all_weights[:, :, :, j * nb : (j + 1) * nb]
        prev = jnp.concatenate([left, block[:, :-1]], axis=1).astype(jnp.float32)
        nxt = jnp.concatenate([block[:, 1:], right], axis=1).astype(jnp.float32)
        total = weights[0] * prev + weights[1] * block.astype(jnp.float32) + weights[2] * nxt
        virtual = total.astype(jnp.bfloat16).reshape(cycles * sector * nb, length)
        spectra = lax.dot_general(
            table, virtual, (((0,), (1,)), ((), ())), preferred_element_type=jnp.float32
        ).astype(jnp.bfloat16)
        spectra = spectra.reshape(2, n_tm, fl, cycles * sector * nb).transpose(1, 0, 2, 3)
        shared = lax.all_to_all(spectra, "tm", 0, 0, tiled=True)
        x = shared.reshape(n_tm, 2, fl, cycles, sector, nb).transpose(2, 4, 3, 0, 1, 5)
        x = x.reshape(fl, local_rows, n_tm, 2, nb)
        rows = x.reshape(fl, local_rows, n_tm * 2 * nb)
        turned = jnp.stack([x[:, :, :, 1], -x[:, :, :, 0]], 3).reshape(rows.shape)
        lhs = jnp.stack([rows, turned], 1)
        columns = lax.all_gather(rows, "az", axis=1, tiled=True)
        part = jnp.einsum("fcqk,fpk->fcqp", lhs, columns, preferred_element_type=jnp.float32)
        result = part if result is None else result + part
    return result * (1.0 / (n_tm * blocks))


def solution(mesh):
    return jax.shard_map(
        shards,
        mesh=mesh,
        in_specs=(P(None, "az", "tm", None), P("tm", None), P("tm", None)),
        out_specs=P("tm", None, "az", None),
        check_vma=False,
    )
```

```python
import math

import jax
import jax.numpy as jnp
from jax import lax
from jax.sharding import PartitionSpec as P

FREQS = 256
BLOCK_CHUNKS = 1


def dft_table(length, freqs):
    step = 64
    bins = jnp.arange(1, freqs + 1, dtype=jnp.int32)
    high = jnp.arange(length // step, dtype=jnp.int32)
    low = jnp.arange(step, dtype=jnp.int32)
    scale = 2.0 * math.pi / length
    a = (high[:, None] * step * bins[None, :] % length).astype(jnp.float32) * scale
    b = (low[:, None] * bins[None, :] % length).astype(jnp.float32) * scale
    ca, sa = jnp.cos(a)[:, None], jnp.sin(a)[:, None]
    cb, sb = jnp.cos(b)[None], jnp.sin(b)[None]
    ca, sa, cb, sb = lax.optimization_barrier((ca, sa, cb, sb))
    cos = (ca * cb - sa * sb).reshape(length, freqs)
    sin = (sa * cb + ca * sb).reshape(length, freqs)
    times = jnp.arange(length, dtype=jnp.int32)
    hann = 0.5 - 0.5 * jnp.cos(times.astype(jnp.float32) * scale)
    factor = hann[:, None] / math.sqrt(3.0 * length / 8.0)
    return jnp.concatenate([factor * cos, -factor * sin], axis=1).astype(jnp.bfloat16)


def interp_weights(offsets, frac):
    rows = []
    for shift in range(-1, 2):
        low = (offsets == shift).astype(frac.dtype)
        high = (offsets + 1 == shift).astype(frac.dtype)
        rows.append((1.0 - frac) * low + frac * high)
    return jnp.stack(rows, 0)


def shards(pressure, offsets, frac):
    cycles, sector, blocks, length = pressure.shape
    subs = offsets.shape[1]
    sub_len = length // subs
    n_az = lax.axis_size("az")
    n_tm = lax.axis_size("tm")
    forward = [(i, (i + 1) % n_az) for i in range(n_az)]
    backward = [((i + 1) % n_az, i) for i in range(n_az)]
    table = dft_table(length, FREQS)
    all_weights = jnp.repeat(interp_weights(offsets, frac), sub_len, axis=2)[:, None, None]
    fl = FREQS // n_tm
    local_rows = sector * cycles
    nb = blocks // BLOCK_CHUNKS
    result = None
    for j in range(BLOCK_CHUNKS):
        block = pressure[:, :, j * nb : (j + 1) * nb]
        left = lax.ppermute(block[:, sector - 1 :], "az", forward)
        right = lax.ppermute(block[:, :1], "az", backward)
        weights = all_weights[:, :, :, j * nb : (j + 1) * nb]
        prev = jnp.concatenate([left, block[:, :-1]], axis=1).astype(jnp.float32)
        nxt = jnp.concatenate([block[:, 1:], right], axis=1).astype(jnp.float32)
        total = weights[0] * prev + weights[1] * block.astype(jnp.float32) + weights[2] * nxt
        virtual = total.astype(jnp.bfloat16).reshape(cycles * sector * nb, length)
        spectra = lax.dot_general(
            table, virtual, (((0,), (1,)), ((), ())), preferred_element_type=jnp.float32
        ).astype(jnp.bfloat16)
        spectra = spectra.reshape(2, n_tm, fl, cycles * sector * nb).transpose(1, 0, 2, 3)
        shared = lax.all_to_all(spectra, "tm", 0, 0, tiled=True)
        x = shared.reshape(n_tm, 2, fl, cycles, sector, nb).transpose(2, 4, 3, 0, 1, 5)
        x = x.reshape(fl, local_rows, n_tm, 2, nb)
        rows = x.reshape(fl, local_rows, n_tm * 2 * nb)
        turned = jnp.stack([x[:, :, :, 1], -x[:, :, :, 0]], 3).reshape(rows.shape)
        lhs = jnp.stack([rows, turned], 1)
        columns = lax.all_gather(rows, "az", axis=1, tiled=True)
        part = jnp.einsum("fcqk,fpk->fcqp", lhs, columns, preferred_element_type=jnp.float32)
        result = part if result is None else result + part
    return result * (1.0 / (n_tm * blocks))


def solution(mesh):
    return jax.shard_map(
        shards,
        mesh=mesh,
        in_specs=(P(None, "az", "tm", None), P("tm", None), P("tm", None)),
        out_specs=P("tm", None, "az", None),
        check_vma=False,
    )
```

```python
import math

import jax
import jax.numpy as jnp
from jax import lax
from jax.sharding import PartitionSpec as P

FREQS = 256
BLOCK_CHUNKS = 1


def dft_table(length, freqs):
    step = 64
    bins = jnp.arange(1, freqs + 1, dtype=jnp.int32)
    high = jnp.arange(length // step, dtype=jnp.int32)
    low = jnp.arange(step, dtype=jnp.int32)
    scale = 2.0 * math.pi / length
    a = (high[:, None] * step * bins[None, :] % length).astype(jnp.float32) * scale
    b = (low[:, None] * bins[None, :] % length).astype(jnp.float32) * scale
    ca, sa = jnp.cos(a)[:, None], jnp.sin(a)[:, None]
    cb, sb = jnp.cos(b)[None], jnp.sin(b)[None]
    ca, sa, cb, sb = lax.optimization_barrier((ca, sa, cb, sb))
    cos = (ca * cb - sa * sb).reshape(length, freqs)
    sin = (sa * cb + ca * sb).reshape(length, freqs)
    times = jnp.arange(length, dtype=jnp.int32)
    hann = 0.5 - 0.5 * jnp.cos(times.astype(jnp.float32) * scale)
    factor = hann[:, None] / math.sqrt(3.0 * length / 8.0)
    return jnp.concatenate([factor * cos, -factor * sin], axis=1).astype(jnp.bfloat16)


def interp_weights(offsets, frac):
    rows = []
    for shift in range(-1, 2):
        low = (offsets == shift).astype(frac.dtype)
        high = (offsets + 1 == shift).astype(frac.dtype)
        rows.append((1.0 - frac) * low + frac * high)
    return jnp.stack(rows, 0)


def shards(pressure, offsets, frac):
    cycles, sector, blocks, length = pressure.shape
    subs = offsets.shape[1]
    sub_len = length // subs
    n_az = lax.axis_size("az")
    n_tm = lax.axis_size("tm")
    forward = [(i, (i + 1) % n_az) for i in range(n_az)]
    backward = [((i + 1) % n_az, i) for i in range(n_az)]
    table = dft_table(length, FREQS)
    all_weights = jnp.repeat(interp_weights(offsets, frac), sub_len, axis=2)[:, None, None]
    fl = FREQS // n_tm
    local_rows = sector * cycles
    nb = blocks // BLOCK_CHUNKS
    result = None
    for j in range(BLOCK_CHUNKS):
        block = pressure[:, :, j * nb : (j + 1) * nb]
        weights = all_weights[:, :, :, j * nb : (j + 1) * nb]

        def transform(v):
            rows = v.astype(jnp.bfloat16).reshape(-1, length)
            return lax.dot_general(
                table, rows, (((0,), (1,)), ((), ())), preferred_element_type=jnp.float32
            )

        to_next = transform(weights[0] * block[:, sector - 1 :].astype(jnp.float32))
        to_prev = transform(weights[2] * block[:, :1].astype(jnp.float32))
        from_prev = lax.ppermute(to_next, "az", forward).reshape(2 * FREQS, cycles, 1, nb)
        from_next = lax.ppermute(to_prev, "az", backward).reshape(2 * FREQS, cycles, 1, nb)
        zero = jnp.zeros_like(block[:, :1])
        prev = jnp.concatenate([zero, block[:, :-1]], axis=1).astype(jnp.float32)
        nxt = jnp.concatenate([block[:, 1:], zero], axis=1).astype(jnp.float32)
        total = weights[0] * prev + weights[1] * block.astype(jnp.float32) + weights[2] * nxt
        inner = transform(total).reshape(2 * FREQS, cycles, sector, nb)
        edges = jnp.concatenate(
            [from_prev, jnp.zeros((2 * FREQS, cycles, sector - 2, nb), jnp.float32), from_next], axis=2
        )
        spectra = (inner + edges).astype(jnp.bfloat16)
        spectra = spectra.reshape(2, n_tm, fl, cycles * sector * nb).transpose(1, 0, 2, 3)
        shared = lax.all_to_all(spectra, "tm", 0, 0, tiled=True)
        x = shared.reshape(n_tm, 2, fl, cycles, sector, nb).transpose(2, 4, 3, 0, 1, 5)
        x = x.reshape(fl, local_rows, n_tm, 2, nb)
        rows = x.reshape(fl, local_rows, n_tm * 2 * nb)
        turned = jnp.stack([x[:, :, :, 1], -x[:, :, :, 0]], 3).reshape(rows.shape)
        lhs = jnp.stack([rows, turned], 1)
        columns = lax.all_gather(rows, "az", axis=1, tiled=True)
        part = jnp.einsum("fcqk,fpk->fcqp", lhs, columns, preferred_element_type=jnp.float32)
        result = part if result is None else result + part
    return result * (1.0 / (n_tm * blocks))


def solution(mesh):
    return jax.shard_map(
        shards,
        mesh=mesh,
        in_specs=(P(None, "az", "tm", None), P("tm", None), P("tm", None)),
        out_specs=P("tm", None, "az", None),
        check_vma=False,
    )
```

```python
import math

import jax
import jax.numpy as jnp
from jax import lax
from jax.sharding import PartitionSpec as P

FREQS = 256
BLOCK_CHUNKS = 1


def dft_table(length, freqs):
    step = 64
    bins = jnp.arange(1, freqs + 1, dtype=jnp.int32)
    high = jnp.arange(length // step, dtype=jnp.int32)
    low = jnp.arange(step, dtype=jnp.int32)
    scale = 2.0 * math.pi / length
    a = (high[:, None] * step * bins[None, :] % length).astype(jnp.float32) * scale
    b = (low[:, None] * bins[None, :] % length).astype(jnp.float32) * scale
    ca, sa = jnp.cos(a)[:, None], jnp.sin(a)[:, None]
    cb, sb = jnp.cos(b)[None], jnp.sin(b)[None]
    ca, sa, cb, sb = lax.optimization_barrier((ca, sa, cb, sb))
    cos = (ca * cb - sa * sb).reshape(length, freqs)
    sin = (sa * cb + ca * sb).reshape(length, freqs)
    times = jnp.arange(length, dtype=jnp.int32)
    hann = 0.5 - 0.5 * jnp.cos(times.astype(jnp.float32) * scale)
    factor = hann[:, None] / math.sqrt(3.0 * length / 8.0)
    return jnp.concatenate([factor * cos, -factor * sin], axis=1).astype(jnp.bfloat16)


def interp_weights(offsets, frac):
    rows = []
    for shift in range(-1, 2):
        low = (offsets == shift).astype(frac.dtype)
        high = (offsets + 1 == shift).astype(frac.dtype)
        rows.append((1.0 - frac) * low + frac * high)
    return jnp.stack(rows, 0)


def shards(pressure, offsets, frac):
    cycles, sector, blocks, length = pressure.shape
    subs = offsets.shape[1]
    sub_len = length // subs
    n_az = lax.axis_size("az")
    n_tm = lax.axis_size("tm")
    forward = [(i, (i + 1) % n_az) for i in range(n_az)]
    backward = [((i + 1) % n_az, i) for i in range(n_az)]
    table = dft_table(length, FREQS)
    all_weights = jnp.repeat(interp_weights(offsets, frac), sub_len, axis=2)[:, None, None]
    fl = FREQS // n_tm
    local_rows = sector * cycles
    nb = blocks // BLOCK_CHUNKS
    result = None
    for j in range(BLOCK_CHUNKS):
        block = pressure[:, :, j * nb : (j + 1) * nb]
        weights = all_weights[:, :, :, j * nb : (j + 1) * nb]

        def transform(v):
            rows = v.astype(jnp.bfloat16).reshape(-1, length)
            return lax.dot_general(
                table, rows, (((0,), (1,)), ((), ())), preferred_element_type=jnp.float32
            )

        to_next = transform(weights[0] * block[:, sector - 1 :].astype(jnp.float32))
        to_prev = transform(weights[2] * block[:, :1].astype(jnp.float32))
        from_prev = lax.ppermute(to_next, "az", forward).reshape(2 * FREQS, cycles, 1, nb)
        from_next = lax.ppermute(to_prev, "az", backward).reshape(2 * FREQS, cycles, 1, nb)
        zero = jnp.zeros_like(block[:, :1])
        prev = jnp.concatenate([zero, block[:, :-1]], axis=1).astype(jnp.float32)
        nxt = jnp.concatenate([block[:, 1:], zero], axis=1).astype(jnp.float32)
        total = weights[0] * prev + weights[1] * block.astype(jnp.float32) + weights[2] * nxt
        inner = transform(total).reshape(2 * FREQS, cycles, sector, nb)
        edges = jnp.concatenate(
            [from_prev, jnp.zeros((2 * FREQS, cycles, sector - 2, nb), jnp.float32), from_next], axis=2
        )
        spectra = (inner + edges).astype(jnp.bfloat16)
        spectra = spectra.reshape(2, n_tm, fl, cycles * sector * nb).transpose(1, 0, 2, 3)
        me = lax.axis_index("tm")
        pieces = [lax.dynamic_index_in_dim(spectra, me, 0, keepdims=False)]
        for s in range(1, n_tm):
            piece = lax.dynamic_index_in_dim(spectra, (me + s) % n_tm, 0, keepdims=False)
            pieces.append(lax.ppermute(piece, "tm", [(i, (i + s) % n_tm) for i in range(n_tm)]))
        shared = jnp.stack(pieces, 0)
        x = shared.reshape(n_tm, 2, fl, cycles, sector, nb).transpose(2, 4, 3, 0, 1, 5)
        x = x.reshape(fl, local_rows, n_tm, 2, nb)
        rows = x.reshape(fl, local_rows, n_tm * 2 * nb)
        turned = jnp.stack([x[:, :, :, 1], -x[:, :, :, 0]], 3).reshape(rows.shape)
        lhs = jnp.stack([rows, turned], 1)
        columns = lax.all_gather(rows, "az", axis=1, tiled=True)
        part = jnp.einsum("fcqk,fpk->fcqp", lhs, columns, preferred_element_type=jnp.float32)
        result = part if result is None else result + part
    return result * (1.0 / (n_tm * blocks))


def solution(mesh):
    return jax.shard_map(
        shards,
        mesh=mesh,
        in_specs=(P(None, "az", "tm", None), P("tm", None), P("tm", None)),
        out_specs=P("tm", None, "az", None),
        check_vma=False,
    )
```

```python
import math

import jax
import jax.numpy as jnp
from jax import lax
from jax.sharding import PartitionSpec as P

FREQS = 256
BLOCK_CHUNKS = 1


def dft_table(length, freqs):
    step = 64
    bins = jnp.arange(1, freqs + 1, dtype=jnp.int32)
    high = jnp.arange(length // step, dtype=jnp.int32)
    low = jnp.arange(step, dtype=jnp.int32)
    scale = 2.0 * math.pi / length
    a = (high[:, None] * step * bins[None, :] % length).astype(jnp.float32) * scale
    b = (low[:, None] * bins[None, :] % length).astype(jnp.float32) * scale
    ca, sa = jnp.cos(a)[:, None], jnp.sin(a)[:, None]
    cb, sb = jnp.cos(b)[None], jnp.sin(b)[None]
    ca, sa, cb, sb = lax.optimization_barrier((ca, sa, cb, sb))
    cos = (ca * cb - sa * sb).reshape(length, freqs)
    sin = (sa * cb + ca * sb).reshape(length, freqs)
    times = jnp.arange(length, dtype=jnp.int32)
    hann = 0.5 - 0.5 * jnp.cos(times.astype(jnp.float32) * scale)
    factor = hann[:, None] / math.sqrt(3.0 * length / 8.0)
    return jnp.concatenate([factor * cos, -factor * sin], axis=1).astype(jnp.bfloat16)


def interp_weights(offsets, frac):
    rows = []
    for shift in range(-1, 2):
        low = (offsets == shift).astype(frac.dtype)
        high = (offsets + 1 == shift).astype(frac.dtype)
        rows.append((1.0 - frac) * low + frac * high)
    return jnp.stack(rows, 0)


def shards(pressure, offsets, frac):
    cycles, sector, blocks, length = pressure.shape
    subs = offsets.shape[1]
    sub_len = length // subs
    n_az = lax.axis_size("az")
    n_tm = lax.axis_size("tm")
    forward = [(i, (i + 1) % n_az) for i in range(n_az)]
    backward = [((i + 1) % n_az, i) for i in range(n_az)]
    table = dft_table(length, FREQS)
    all_weights = jnp.repeat(interp_weights(offsets, frac), sub_len, axis=2)[:, None, None]
    fl = FREQS // n_tm
    local_rows = sector * cycles
    nb = blocks // BLOCK_CHUNKS
    result = None
    for j in range(BLOCK_CHUNKS):
        block = pressure[:, :, j * nb : (j + 1) * nb]
        weights = all_weights[:, :, :, j * nb : (j + 1) * nb]

        def transform(v):
            rows = v.astype(jnp.bfloat16).reshape(-1, length)
            return lax.dot_general(
                table, rows, (((0,), (1,)), ((), ())), preferred_element_type=jnp.float32
            )

        to_next = transform(weights[0] * block[:, sector - 1 :].astype(jnp.float32))
        to_prev = transform(weights[2] * block[:, :1].astype(jnp.float32))
        from_prev = lax.ppermute(to_next, "az", forward).reshape(2 * FREQS, cycles, 1, nb)
        from_next = lax.ppermute(to_prev, "az", backward).reshape(2 * FREQS, cycles, 1, nb)
        zero = jnp.zeros_like(block[:, :1])
        prev = jnp.concatenate([zero, block[:, :-1]], axis=1).astype(jnp.float32)
        nxt = jnp.concatenate([block[:, 1:], zero], axis=1).astype(jnp.float32)
        total = weights[0] * prev + weights[1] * block.astype(jnp.float32) + weights[2] * nxt
        inner = lax.optimization_barrier(transform(total))
        edges = jnp.concatenate(
            [from_prev, jnp.zeros((2 * FREQS, cycles, sector - 2, nb), jnp.float32), from_next], axis=2
        )
        spectra = (inner + edges.reshape(inner.shape)).astype(jnp.bfloat16)
        spectra = spectra.reshape(2, n_tm, fl, cycles * sector * nb).transpose(1, 0, 2, 3)
        shared = lax.all_to_all(spectra, "tm", 0, 0, tiled=True)
        x = shared.reshape(n_tm, 2, fl, cycles, sector, nb).transpose(2, 4, 3, 0, 1, 5)
        x = x.reshape(fl, local_rows, n_tm, 2, nb)
        rows = x.reshape(fl, local_rows, n_tm * 2 * nb)
        turned = jnp.stack([x[:, :, :, 1], -x[:, :, :, 0]], 3).reshape(rows.shape)
        lhs = jnp.stack([rows, turned], 1)
        columns = lax.all_gather(rows, "az", axis=1, tiled=True)
        part = jnp.einsum("fcqk,fpk->fcqp", lhs, columns, preferred_element_type=jnp.float32)
        result = part if result is None else result + part
    return result * (1.0 / (n_tm * blocks))


def solution(mesh):
    return jax.shard_map(
        shards,
        mesh=mesh,
        in_specs=(P(None, "az", "tm", None), P("tm", None), P("tm", None)),
        out_specs=P("tm", None, "az", None),
        check_vma=False,
    )
```

```python
import math

import jax
import jax.numpy as jnp
from jax import lax
from jax.sharding import PartitionSpec as P

FREQS = 256
BLOCK_CHUNKS = 1


def dft_table(length, freqs):
    step = 64
    bins = jnp.arange(1, freqs + 1, dtype=jnp.int32)
    high = jnp.arange(length // step, dtype=jnp.int32)
    low = jnp.arange(step, dtype=jnp.int32)
    scale = 2.0 * math.pi / length
    a = (high[:, None] * step * bins[None, :] % length).astype(jnp.float32) * scale
    b = (low[:, None] * bins[None, :] % length).astype(jnp.float32) * scale
    ca, sa = jnp.cos(a)[:, None], jnp.sin(a)[:, None]
    cb, sb = jnp.cos(b)[None], jnp.sin(b)[None]
    ca, sa, cb, sb = lax.optimization_barrier((ca, sa, cb, sb))
    cos = (ca * cb - sa * sb).reshape(length, freqs)
    sin = (sa * cb + ca * sb).reshape(length, freqs)
    times = jnp.arange(length, dtype=jnp.int32)
    hann = 0.5 - 0.5 * jnp.cos(times.astype(jnp.float32) * scale)
    factor = hann[:, None] / math.sqrt(3.0 * length / 8.0)
    return jnp.concatenate([factor * cos, -factor * sin], axis=1).astype(jnp.bfloat16)


def interp_weights(offsets, frac):
    rows = []
    for shift in range(-1, 2):
        low = (offsets == shift).astype(frac.dtype)
        high = (offsets + 1 == shift).astype(frac.dtype)
        rows.append((1.0 - frac) * low + frac * high)
    return jnp.stack(rows, 0)


def shards(pressure, offsets, frac):
    cycles, sector, blocks, length = pressure.shape
    subs = offsets.shape[1]
    sub_len = length // subs
    n_az = lax.axis_size("az")
    n_tm = lax.axis_size("tm")
    forward = [(i, (i + 1) % n_az) for i in range(n_az)]
    backward = [((i + 1) % n_az, i) for i in range(n_az)]
    table = dft_table(length, FREQS)
    all_weights = jnp.repeat(interp_weights(offsets, frac), sub_len, axis=2)[:, None, None]
    fl = FREQS // n_tm
    local_rows = sector * cycles
    nb = blocks // BLOCK_CHUNKS
    result = None
    for j in range(BLOCK_CHUNKS):
        block = pressure[:, :, j * nb : (j + 1) * nb]
        weights = all_weights[:, :, :, j * nb : (j + 1) * nb]

        def transform(v):
            rows = v.astype(jnp.bfloat16).reshape(-1, length)
            return lax.dot_general(
                table, rows, (((0,), (1,)), ((), ())), preferred_element_type=jnp.float32
            )

        to_next = transform(weights[0] * block[:, sector - 1 :].astype(jnp.float32))
        to_prev = transform(weights[2] * block[:, :1].astype(jnp.float32))
        from_prev = lax.ppermute(to_next, "az", forward).reshape(2 * FREQS, 1, cycles, nb)
        from_next = lax.ppermute(to_prev, "az", backward).reshape(2 * FREQS, 1, cycles, nb)
        zero = jnp.zeros_like(block[:, :1])
        prev = jnp.concatenate([zero, block[:, :-1]], axis=1).astype(jnp.float32)
        nxt = jnp.concatenate([block[:, 1:], zero], axis=1).astype(jnp.float32)
        total = weights[0] * prev + weights[1] * block.astype(jnp.float32) + weights[2] * nxt
        inner = lax.optimization_barrier(transform(total.transpose(1, 0, 2, 3)))
        edges = jnp.concatenate(
            [from_prev, jnp.zeros((2 * FREQS, sector - 2, cycles, nb), jnp.float32), from_next], axis=1
        )
        spectra = (inner + edges.reshape(inner.shape)).astype(jnp.bfloat16)
        spectra = spectra.reshape(2, n_tm, fl, cycles * sector * nb).transpose(1, 0, 2, 3)
        shared = lax.all_to_all(spectra, "tm", 0, 0, tiled=True)
        x = shared.reshape(n_tm, 2, fl, local_rows, nb).transpose(2, 3, 0, 1, 4)
        x = x.reshape(fl, local_rows, n_tm, 2, nb)
        rows = x.reshape(fl, local_rows, n_tm * 2 * nb)
        turned = jnp.stack([x[:, :, :, 1], -x[:, :, :, 0]], 3).reshape(rows.shape)
        lhs = jnp.stack([rows, turned], 1)
        columns = lax.all_gather(rows, "az", axis=1, tiled=True)
        part = jnp.einsum("fcqk,fpk->fcqp", lhs, columns, preferred_element_type=jnp.float32)
        result = part if result is None else result + part
    return result * (1.0 / (n_tm * blocks))


def solution(mesh):
    return jax.shard_map(
        shards,
        mesh=mesh,
        in_specs=(P(None, "az", "tm", None), P("tm", None), P("tm", None)),
        out_specs=P("tm", None, "az", None),
        check_vma=False,
    )
```

```python
import math

import jax
import jax.numpy as jnp
from jax import lax
from jax.sharding import PartitionSpec as P

FREQS = 256
BLOCK_CHUNKS = 1


def dft_table(length, freqs):
    step = 64
    bins = jnp.arange(1, freqs + 1, dtype=jnp.int32)
    high = jnp.arange(length // step, dtype=jnp.int32)
    low = jnp.arange(step, dtype=jnp.int32)
    scale = 2.0 * math.pi / length
    a = (high[:, None] * step * bins[None, :] % length).astype(jnp.float32) * scale
    b = (low[:, None] * bins[None, :] % length).astype(jnp.float32) * scale
    ca, sa = jnp.cos(a)[:, None], jnp.sin(a)[:, None]
    cb, sb = jnp.cos(b)[None], jnp.sin(b)[None]
    ca, sa, cb, sb = lax.optimization_barrier((ca, sa, cb, sb))
    cos = (ca * cb - sa * sb).reshape(length, freqs)
    sin = (sa * cb + ca * sb).reshape(length, freqs)
    times = jnp.arange(length, dtype=jnp.int32)
    hann = 0.5 - 0.5 * jnp.cos(times.astype(jnp.float32) * scale)
    factor = hann[:, None] / math.sqrt(3.0 * length / 8.0)
    return jnp.concatenate([factor * cos, -factor * sin], axis=1).astype(jnp.bfloat16)


def interp_weights(offsets, frac):
    rows = []
    for shift in range(-1, 2):
        low = (offsets == shift).astype(frac.dtype)
        high = (offsets + 1 == shift).astype(frac.dtype)
        rows.append((1.0 - frac) * low + frac * high)
    return jnp.stack(rows, 0)


def shards(pressure, offsets, frac):
    cycles, sector, blocks, length = pressure.shape
    subs = offsets.shape[1]
    sub_len = length // subs
    n_az = lax.axis_size("az")
    n_tm = lax.axis_size("tm")
    forward = [(i, (i + 1) % n_az) for i in range(n_az)]
    backward = [((i + 1) % n_az, i) for i in range(n_az)]
    table = dft_table(length, FREQS)
    all_weights = jnp.repeat(interp_weights(offsets, frac), sub_len, axis=2)[:, None, None]
    fl = FREQS // n_tm
    local_rows = sector * cycles
    nb = blocks // BLOCK_CHUNKS
    result = None
    for j in range(BLOCK_CHUNKS):
        block = pressure[:, :, j * nb : (j + 1) * nb]
        weights = all_weights[:, :, :, j * nb : (j + 1) * nb]

        def transform(v):
            rows = v.astype(jnp.bfloat16).reshape(-1, length)
            return lax.dot_general(
                table, rows, (((0,), (1,)), ((), ())), preferred_element_type=jnp.float32
            )

        to_next = transform(weights[0] * block[:, sector - 1 :].astype(jnp.float32))
        to_prev = transform(weights[2] * block[:, :1].astype(jnp.float32))
        from_prev = lax.ppermute(to_next, "az", forward)
        from_next = lax.ppermute(to_prev, "az", backward)
        zero = jnp.zeros_like(block[:, :1])
        prev = jnp.concatenate([zero, block[:, :-1]], axis=1).astype(jnp.float32)
        nxt = jnp.concatenate([block[:, 1:], zero], axis=1).astype(jnp.float32)
        total = weights[0] * prev + weights[1] * block.astype(jnp.float32) + weights[2] * nxt
        inner = lax.optimization_barrier(transform(total.transpose(1, 0, 2, 3)))
        run = cycles * nb
        spectra = jnp.concatenate(
            [inner[:, :run] + from_prev, inner[:, run:-run], inner[:, -run:] + from_next], axis=1
        ).astype(jnp.bfloat16)
        spectra = spectra.reshape(2, n_tm, fl, cycles * sector * nb).transpose(1, 0, 2, 3)
        shared = lax.all_to_all(spectra, "tm", 0, 0, tiled=True)
        x = shared.reshape(n_tm, 2, fl, local_rows, nb).transpose(2, 3, 0, 1, 4)
        x = x.reshape(fl, local_rows, n_tm, 2, nb)
        rows = x.reshape(fl, local_rows, n_tm * 2 * nb)
        turned = jnp.stack([x[:, :, :, 1], -x[:, :, :, 0]], 3).reshape(rows.shape)
        lhs = jnp.stack([rows, turned], 1)
        columns = lax.all_gather(rows, "az", axis=1, tiled=True)
        part = jnp.einsum("fcqk,fpk->fcqp", lhs, columns, preferred_element_type=jnp.float32)
        result = part if result is None else result + part
    return result * (1.0 / (n_tm * blocks))


def solution(mesh):
    return jax.shard_map(
        shards,
        mesh=mesh,
        in_specs=(P(None, "az", "tm", None), P("tm", None), P("tm", None)),
        out_specs=P("tm", None, "az", None),
        check_vma=False,
    )
```

```python
import math

import jax
import jax.numpy as jnp
from jax import lax
from jax.sharding import Mesh
from jax.sharding import PartitionSpec as P

FREQS = 256
BLOCK_CHUNKS = 1
AZ = ("xh", "z", "core")
TM = ("xl", "y")
CHIPS = ("xh", "z")


def dft_table(length, freqs):
    step = 64
    bins = jnp.arange(1, freqs + 1, dtype=jnp.int32)
    high = jnp.arange(length // step, dtype=jnp.int32)
    low = jnp.arange(step, dtype=jnp.int32)
    scale = 2.0 * math.pi / length
    a = (high[:, None] * step * bins[None, :] % length).astype(jnp.float32) * scale
    b = (low[:, None] * bins[None, :] % length).astype(jnp.float32) * scale
    ca, sa = jnp.cos(a)[:, None], jnp.sin(a)[:, None]
    cb, sb = jnp.cos(b)[None], jnp.sin(b)[None]
    ca, sa, cb, sb = lax.optimization_barrier((ca, sa, cb, sb))
    cos = (ca * cb - sa * sb).reshape(length, freqs)
    sin = (sa * cb + ca * sb).reshape(length, freqs)
    times = jnp.arange(length, dtype=jnp.int32)
    hann = 0.5 - 0.5 * jnp.cos(times.astype(jnp.float32) * scale)
    factor = hann[:, None] / math.sqrt(3.0 * length / 8.0)
    return jnp.concatenate([factor * cos, -factor * sin], axis=1).astype(jnp.bfloat16)


def interp_weights(offsets, frac):
    rows = []
    for shift in range(-1, 2):
        low = (offsets == shift).astype(frac.dtype)
        high = (offsets + 1 == shift).astype(frac.dtype)
        rows.append((1.0 - frac) * low + frac * high)
    return jnp.stack(rows, 0)


def shards(pressure, offsets, frac):
    cycles, sector, blocks, length = pressure.shape
    subs = offsets.shape[1]
    sub_len = length // subs
    n_az = lax.axis_size(AZ)
    n_tm = lax.axis_size(TM)
    forward = [(i, (i + 1) % n_az) for i in range(n_az)]
    backward = [((i + 1) % n_az, i) for i in range(n_az)]
    table = dft_table(length, FREQS)
    all_weights = jnp.repeat(interp_weights(offsets, frac), sub_len, axis=2)[:, None, None]
    fl = FREQS // n_tm
    local_rows = sector * cycles
    nb = blocks // BLOCK_CHUNKS
    result = None
    for j in range(BLOCK_CHUNKS):
        block = pressure[:, :, j * nb : (j + 1) * nb]
        weights = all_weights[:, :, :, j * nb : (j + 1) * nb]

        def transform(v):
            rows = v.astype(jnp.bfloat16).reshape(-1, length)
            return lax.dot_general(
                table, rows, (((0,), (1,)), ((), ())), preferred_element_type=jnp.float32
            )

        to_next = transform(weights[0] * block[:, sector - 1 :].astype(jnp.float32))
        to_prev = transform(weights[2] * block[:, :1].astype(jnp.float32))
        from_prev = lax.ppermute(to_next, AZ, forward)
        from_next = lax.ppermute(to_prev, AZ, backward)
        zero = jnp.zeros_like(block[:, :1])
        prev = jnp.concatenate([zero, block[:, :-1]], axis=1).astype(jnp.float32)
        nxt = jnp.concatenate([block[:, 1:], zero], axis=1).astype(jnp.float32)
        total = weights[0] * prev + weights[1] * block.astype(jnp.float32) + weights[2] * nxt
        inner = lax.optimization_barrier(transform(total.transpose(1, 0, 2, 3)))
        run = cycles * nb
        spectra = jnp.concatenate(
            [inner[:, :run] + from_prev, inner[:, run:-run], inner[:, -run:] + from_next], axis=1
        ).astype(jnp.bfloat16)
        spectra = spectra.reshape(2, n_tm, fl, cycles * sector * nb).transpose(1, 0, 2, 3)
        shared = lax.all_to_all(spectra, TM, 0, 0, tiled=True)
        x = shared.reshape(n_tm, 2, fl, local_rows, nb).transpose(2, 3, 0, 1, 4)
        x = x.reshape(fl, local_rows, n_tm, 2, nb)
        rows = x.reshape(fl, local_rows, n_tm * 2 * nb)
        turned = jnp.stack([x[:, :, :, 1], -x[:, :, :, 0]], 3).reshape(rows.shape)
        lhs = jnp.stack([rows, turned], 1).reshape(fl, 2, local_rows, n_tm, 2, nb)
        core = lax.axis_index("core")
        swap = [(0, 1), (1, 0)]
        x = x.reshape(fl, local_rows, n_tm, 2, nb)
        mine = lax.dynamic_index_in_dim(x, core, 3, keepdims=False)
        theirs = lax.ppermute(lax.dynamic_index_in_dim(x, 1 - core, 3, keepdims=False), "core", swap)
        chip = jnp.where(
            core == 0, jnp.concatenate([mine, theirs], 1), jnp.concatenate([theirs, mine], 1)
        ).reshape(fl, 2 * local_rows, n_tm * nb)
        own_cols = lax.all_gather(chip, CHIPS, axis=1, tiled=True)
        other_cols = lax.ppermute(own_cols, "core", swap)
        l_own = lax.dynamic_index_in_dim(lhs, core, 4, keepdims=False).reshape(fl, 2, local_rows, -1)
        l_other = lax.dynamic_index_in_dim(lhs, 1 - core, 4, keepdims=False).reshape(fl, 2, local_rows, -1)
        part = jnp.einsum(
            "fcqk,fpk->fcqp", l_own, own_cols, preferred_element_type=jnp.float32
        ) + jnp.einsum("fcqk,fpk->fcqp", l_other, other_cols, preferred_element_type=jnp.float32)
        result = part if result is None else result + part
    return result * (1.0 / (n_tm * blocks))


def solution(mesh):
    az, tm = mesh.devices.shape
    fine = Mesh(mesh.devices.reshape(2, az // 4, 2, 2, tm // 2), ("xh", "z", "core", "xl", "y"))
    return jax.shard_map(
        shards,
        mesh=fine,
        in_specs=(P(None, AZ, TM, None), P(TM, None), P(TM, None)),
        out_specs=P(TM, None, AZ, None),
        check_vma=False,
    )
```

```python
import functools
import math

import jax
import jax.numpy as jnp
from jax import lax
from jax.experimental import pallas as pl
from jax.experimental.pallas import tpu as pltpu
from jax.sharding import PartitionSpec as P

FREQS = 256
BLOCK_CHUNKS = 1


def dft_table(length, freqs):
    step = 64
    bins = jnp.arange(1, freqs + 1, dtype=jnp.int32)
    high = jnp.arange(length // step, dtype=jnp.int32)
    low = jnp.arange(step, dtype=jnp.int32)
    scale = 2.0 * math.pi / length
    a = (high[:, None] * step * bins[None, :] % length).astype(jnp.float32) * scale
    b = (low[:, None] * bins[None, :] % length).astype(jnp.float32) * scale
    ca, sa = jnp.cos(a)[:, None], jnp.sin(a)[:, None]
    cb, sb = jnp.cos(b)[None], jnp.sin(b)[None]
    ca, sa, cb, sb = lax.optimization_barrier((ca, sa, cb, sb))
    cos = (ca * cb - sa * sb).reshape(length, freqs)
    sin = (sa * cb + ca * sb).reshape(length, freqs)
    times = jnp.arange(length, dtype=jnp.int32)
    hann = 0.5 - 0.5 * jnp.cos(times.astype(jnp.float32) * scale)
    factor = hann[:, None] / math.sqrt(3.0 * length / 8.0)
    return jnp.concatenate([factor * cos, -factor * sin], axis=1).astype(jnp.bfloat16)


def interp_weights(offsets, frac):
    rows = []
    for shift in range(-1, 2):
        low = (offsets == shift).astype(frac.dtype)
        high = (offsets + 1 == shift).astype(frac.dtype)
        rows.append((1.0 - frac) * low + frac * high)
    return jnp.stack(rows, 0)


def csm_kernel(lhs_ref, rhs_ref, out_ref, *, scale):
    for i in range(lhs_ref.shape[0]):
        prod = lax.dot_general(
            lhs_ref[i], rhs_ref[i], (((1,), (1,)), ((), ())), preferred_element_type=jnp.float32
        )
        out_ref[i] = (prod * scale).reshape(out_ref.shape[1:])


def cross_terms(lhs, columns, scale):
    freqs, rows, width = lhs.shape
    mics = columns.shape[1]
    step = 4
    return pl.pallas_call(
        functools.partial(csm_kernel, scale=scale),
        grid=(freqs // step,),
        in_specs=[
            pl.BlockSpec((step, rows, width), lambda i: (i, 0, 0)),
            pl.BlockSpec((step, mics, width), lambda i: (i, 0, 0)),
        ],
        out_specs=pl.BlockSpec((step, 2, rows // 2, mics), lambda i: (i, 0, 0, 0)),
        out_shape=jax.ShapeDtypeStruct((freqs, 2, rows // 2, mics), jnp.float32),
        compiler_params=pltpu.CompilerParams(vmem_limit_bytes=48 * 1024 * 1024),
    )(lhs, columns)


def shards(pressure, offsets, frac):
    cycles, sector, blocks, length = pressure.shape
    subs = offsets.shape[1]
    sub_len = length // subs
    n_az = lax.axis_size("az")
    n_tm = lax.axis_size("tm")
    forward = [(i, (i + 1) % n_az) for i in range(n_az)]
    backward = [((i + 1) % n_az, i) for i in range(n_az)]
    table = dft_table(length, FREQS)
    all_weights = jnp.repeat(interp_weights(offsets, frac), sub_len, axis=2)[:, None, None]
    fl = FREQS // n_tm
    local_rows = sector * cycles
    nb = blocks // BLOCK_CHUNKS
    result = None
    for j in range(BLOCK_CHUNKS):
        block = pressure[:, :, j * nb : (j + 1) * nb]
        weights = all_weights[:, :, :, j * nb : (j + 1) * nb]

        def transform(v):
            rows = v.astype(jnp.bfloat16).reshape(-1, length)
            return lax.dot_general(
                table, rows, (((0,), (1,)), ((), ())), preferred_element_type=jnp.float32
            )

        to_next = transform(weights[0] * block[:, sector - 1 :].astype(jnp.float32))
        to_prev = transform(weights[2] * block[:, :1].astype(jnp.float32))
        from_prev = lax.ppermute(to_next, "az", forward)
        from_next = lax.ppermute(to_prev, "az", backward)
        zero = jnp.zeros_like(block[:, :1])
        prev = jnp.concatenate([zero, block[:, :-1]], axis=1).astype(jnp.float32)
        nxt = jnp.concatenate([block[:, 1:], zero], axis=1).astype(jnp.float32)
        total = weights[0] * prev + weights[1] * block.astype(jnp.float32) + weights[2] * nxt
        inner = lax.optimization_barrier(transform(total.transpose(1, 0, 2, 3)))
        run = cycles * nb
        spectra = jnp.concatenate(
            [inner[:, :run] + from_prev, inner[:, run:-run], inner[:, -run:] + from_next], axis=1
        ).astype(jnp.bfloat16)
        spectra = spectra.reshape(2, n_tm, fl, cycles * sector * nb).transpose(1, 0, 2, 3)
        shared = lax.all_to_all(spectra, "tm", 0, 0, tiled=True)
        x = shared.reshape(n_tm, 2, fl, local_rows, nb).transpose(2, 3, 0, 1, 4)
        x = x.reshape(fl, local_rows, n_tm, 2, nb)
        rows = x.reshape(fl, local_rows, n_tm * 2 * nb)
        turned = jnp.stack([x[:, :, :, 1], -x[:, :, :, 0]], 3).reshape(rows.shape)
        lhs = jnp.stack([rows, turned], 1)
        columns = lax.all_gather(rows, "az", axis=1, tiled=True)
        part = cross_terms(lhs.reshape(fl, 2 * local_rows, -1), columns, 1.0 / (n_tm * blocks))
        result = part if result is None else result + part
    return result


def solution(mesh):
    return jax.shard_map(
        shards,
        mesh=mesh,
        in_specs=(P(None, "az", "tm", None), P("tm", None), P("tm", None)),
        out_specs=P("tm", None, "az", None),
        check_vma=False,
    )
```

```python
import math

import jax
import jax.numpy as jnp
from jax import lax
from jax.sharding import Mesh
from jax.sharding import PartitionSpec as P

FREQS = 256
BLOCK_CHUNKS = 1
AZ = ("xh", "z", "core")
TM = ("xl", "y")


def dft_table(length, freqs):
    step = 64
    bins = jnp.arange(1, freqs + 1, dtype=jnp.int32)
    high = jnp.arange(length // step, dtype=jnp.int32)
    low = jnp.arange(step, dtype=jnp.int32)
    scale = 2.0 * math.pi / length
    a = (high[:, None] * step * bins[None, :] % length).astype(jnp.float32) * scale
    b = (low[:, None] * bins[None, :] % length).astype(jnp.float32) * scale
    ca, sa = jnp.cos(a)[:, None], jnp.sin(a)[:, None]
    cb, sb = jnp.cos(b)[None], jnp.sin(b)[None]
    ca, sa, cb, sb = lax.optimization_barrier((ca, sa, cb, sb))
    cos = (ca * cb - sa * sb).reshape(length, freqs)
    sin = (sa * cb + ca * sb).reshape(length, freqs)
    times = jnp.arange(length, dtype=jnp.int32)
    hann = 0.5 - 0.5 * jnp.cos(times.astype(jnp.float32) * scale)
    factor = hann[:, None] / math.sqrt(3.0 * length / 8.0)
    return jnp.concatenate([factor * cos, -factor * sin], axis=1).astype(jnp.bfloat16)


def interp_weights(offsets, frac):
    rows = []
    for shift in range(-1, 2):
        low = (offsets == shift).astype(frac.dtype)
        high = (offsets + 1 == shift).astype(frac.dtype)
        rows.append((1.0 - frac) * low + frac * high)
    return jnp.stack(rows, 0)


def shards(pressure, offsets, frac):
    cycles, sector, blocks, length = pressure.shape
    subs = offsets.shape[1]
    sub_len = length // subs
    n_az = lax.axis_size(AZ)
    n_tm = lax.axis_size(TM)
    forward = [(i, (i + 1) % n_az) for i in range(n_az)]
    backward = [((i + 1) % n_az, i) for i in range(n_az)]
    table = dft_table(length, FREQS)
    all_weights = jnp.repeat(interp_weights(offsets, frac), sub_len, axis=2)[:, None, None]
    fl = FREQS // n_tm
    local_rows = sector * cycles
    nb = blocks // BLOCK_CHUNKS
    result = None
    for j in range(BLOCK_CHUNKS):
        block = pressure[:, :, j * nb : (j + 1) * nb]
        weights = all_weights[:, :, :, j * nb : (j + 1) * nb]

        def transform(v):
            rows = v.astype(jnp.bfloat16).reshape(-1, length)
            return lax.dot_general(
                table, rows, (((0,), (1,)), ((), ())), preferred_element_type=jnp.float32
            )

        to_next = transform(weights[0] * block[:, sector - 1 :].astype(jnp.float32))
        to_prev = transform(weights[2] * block[:, :1].astype(jnp.float32))
        from_prev = lax.ppermute(to_next, AZ, forward)
        from_next = lax.ppermute(to_prev, AZ, backward)
        zero = jnp.zeros_like(block[:, :1])
        prev = jnp.concatenate([zero, block[:, :-1]], axis=1).astype(jnp.float32)
        nxt = jnp.concatenate([block[:, 1:], zero], axis=1).astype(jnp.float32)
        total = weights[0] * prev + weights[1] * block.astype(jnp.float32) + weights[2] * nxt
        inner = lax.optimization_barrier(transform(total.transpose(1, 0, 2, 3)))
        run = cycles * nb
        spectra = jnp.concatenate(
            [inner[:, :run] + from_prev, inner[:, run:-run], inner[:, -run:] + from_next], axis=1
        ).astype(jnp.bfloat16)
        spectra = spectra.reshape(2, n_tm, fl, cycles * sector * nb).transpose(1, 0, 2, 3)
        shared = spectra.reshape(2, n_tm // 2, *spectra.shape[1:])
        shared = lax.all_to_all(shared, "y", 1, 1, tiled=True)
        shared = lax.all_to_all(shared, "xl", 0, 0, tiled=True).reshape(spectra.shape)
        x = shared.reshape(n_tm, 2, fl, local_rows, nb).transpose(2, 3, 0, 1, 4)
        x = x.reshape(fl, local_rows, n_tm, 2, nb)
        rows = x.reshape(fl, local_rows, n_tm * 2 * nb)
        turned = jnp.stack([x[:, :, :, 1], -x[:, :, :, 0]], 3).reshape(rows.shape)
        lhs = jnp.stack([rows, turned], 1)
        columns = lax.all_gather(rows, AZ, axis=1, tiled=True)
        part = jnp.einsum("fcqk,fpk->fcqp", lhs, columns, preferred_element_type=jnp.float32)
        result = part if result is None else result + part
    return result * (1.0 / (n_tm * blocks))


def solution(mesh):
    az, tm = mesh.devices.shape
    fine = Mesh(mesh.devices.reshape(2, az // 4, 2, 2, tm // 2), ("xh", "z", "core", "xl", "y"))
    return jax.shard_map(
        shards,
        mesh=fine,
        in_specs=(P(None, AZ, TM, None), P(TM, None), P(TM, None)),
        out_specs=P(TM, None, AZ, None),
        check_vma=False,
    )
```

```python
import math

import jax
import jax.numpy as jnp
from jax import lax
from jax.sharding import PartitionSpec as P

FREQS = 256
BLOCK_CHUNKS = 1


def dft_table(length, freqs):
    step = 64
    bins = jnp.arange(1, freqs + 1, dtype=jnp.int32)
    high = jnp.arange(length // step, dtype=jnp.int32)
    low = jnp.arange(step, dtype=jnp.int32)
    scale = 2.0 * math.pi / length
    a = (high[:, None] * step * bins[None, :] % length).astype(jnp.float32) * scale
    b = (low[:, None] * bins[None, :] % length).astype(jnp.float32) * scale
    ca, sa = jnp.cos(a)[:, None], jnp.sin(a)[:, None]
    cb, sb = jnp.cos(b)[None], jnp.sin(b)[None]
    ca, sa, cb, sb = lax.optimization_barrier((ca, sa, cb, sb))
    cos = (ca * cb - sa * sb).reshape(length, freqs)
    sin = (sa * cb + ca * sb).reshape(length, freqs)
    times = jnp.arange(length, dtype=jnp.int32)
    hann = 0.5 - 0.5 * jnp.cos(times.astype(jnp.float32) * scale)
    factor = hann[:, None] / math.sqrt(3.0 * length / 8.0)
    return jnp.concatenate([factor * cos, -factor * sin], axis=1).astype(jnp.bfloat16)


def interp_weights(offsets, frac):
    rows = []
    for shift in range(-1, 2):
        low = (offsets == shift).astype(frac.dtype)
        high = (offsets + 1 == shift).astype(frac.dtype)
        rows.append((1.0 - frac) * low + frac * high)
    return jnp.stack(rows, 0)


def shards(pressure, offsets, frac):
    cycles, sector, blocks, length = pressure.shape
    subs = offsets.shape[1]
    sub_len = length // subs
    n_az = lax.axis_size("az")
    n_tm = lax.axis_size("tm")
    forward = [(i, (i + 1) % n_az) for i in range(n_az)]
    backward = [((i + 1) % n_az, i) for i in range(n_az)]
    table = dft_table(length, FREQS)
    all_weights = jnp.repeat(interp_weights(offsets, frac), sub_len, axis=2)[:, None, None]
    fl = FREQS // n_tm
    local_rows = sector * cycles
    nb = blocks // BLOCK_CHUNKS
    result = None
    for j in range(BLOCK_CHUNKS):
        block = pressure[:, :, j * nb : (j + 1) * nb]
        weights = all_weights[:, :, :, j * nb : (j + 1) * nb]

        def transform(rows):
            return lax.dot_general(
                table, rows.reshape(-1, length), (((0,), (1,)), ((), ())),
                preferred_element_type=jnp.float32,
            )

        def split(v):
            hi = v.astype(jnp.bfloat16)
            return hi, (v - hi.astype(jnp.float32)).astype(jnp.bfloat16)

        def edge(v):
            hi, lo = split(v)
            both = transform(jnp.concatenate([hi, lo], 0))
            return both[:, : both.shape[1] // 2] + both[:, both.shape[1] // 2 :]

        to_next = edge(weights[0] * block[:, sector - 1 :].astype(jnp.float32))
        to_prev = edge(weights[2] * block[:, :1].astype(jnp.float32))
        from_prev = lax.ppermute(to_next, "az", forward)
        from_next = lax.ppermute(to_prev, "az", backward)
        zero = jnp.zeros_like(block[:, :1])
        prev = jnp.concatenate([zero, block[:, :-1]], axis=1).astype(jnp.float32)
        nxt = jnp.concatenate([block[:, 1:], zero], axis=1).astype(jnp.float32)
        total = weights[0] * prev + weights[1] * block.astype(jnp.float32) + weights[2] * nxt
        total = total.transpose(1, 0, 2, 3)
        hi, lo = split(total)
        rest = jnp.concatenate([lo[:1], lo[-1:]], 0)
        inner = lax.optimization_barrier(transform(jnp.concatenate([hi, rest], 0)))
        run = cycles * nb
        body = sector * run
        spectra = jnp.concatenate(
            [
                inner[:, :run] + inner[:, body : body + run] + from_prev,
                inner[:, run : body - run],
                inner[:, body - run : body] + inner[:, body + run :] + from_next,
            ],
            axis=1,
        ).astype(jnp.bfloat16)
        spectra = spectra.reshape(2, n_tm, fl, cycles * sector * nb).transpose(1, 0, 2, 3)
        shared = lax.all_to_all(spectra, "tm", 0, 0, tiled=True)
        x = shared.reshape(n_tm, 2, fl, local_rows, nb).transpose(2, 3, 0, 1, 4)
        x = x.reshape(fl, local_rows, n_tm, 2, nb)
        rows = x.reshape(fl, local_rows, n_tm * 2 * nb)
        turned = jnp.stack([x[:, :, :, 1], -x[:, :, :, 0]], 3).reshape(rows.shape)
        lhs = jnp.stack([rows, turned], 1)
        columns = lax.all_gather(rows, "az", axis=1, tiled=True)
        part = jnp.einsum("fcqk,fpk->fcqp", lhs, columns, preferred_element_type=jnp.float32)
        result = part if result is None else result + part
    return result * (1.0 / (n_tm * blocks))


def solution(mesh):
    return jax.shard_map(
        shards,
        mesh=mesh,
        in_specs=(P(None, "az", "tm", None), P("tm", None), P("tm", None)),
        out_specs=P("tm", None, "az", None),
        check_vma=False,
    )
```

```python
import math

import jax
import jax.numpy as jnp
from jax import lax
from jax.sharding import PartitionSpec as P

FREQS = 256
BLOCK_CHUNKS = 1


def dft_table(length, freqs):
    step = 64
    bins = jnp.arange(1, freqs + 1, dtype=jnp.int32)
    high = jnp.arange(length // step, dtype=jnp.int32)
    low = jnp.arange(step, dtype=jnp.int32)
    scale = 2.0 * math.pi / length
    a = (high[:, None] * step * bins[None, :] % length).astype(jnp.float32) * scale
    b = (low[:, None] * bins[None, :] % length).astype(jnp.float32) * scale
    ca, sa = jnp.cos(a)[:, None], jnp.sin(a)[:, None]
    cb, sb = jnp.cos(b)[None], jnp.sin(b)[None]
    ca, sa, cb, sb = lax.optimization_barrier((ca, sa, cb, sb))
    cos = (ca * cb - sa * sb).reshape(length, freqs)
    sin = (sa * cb + ca * sb).reshape(length, freqs)
    times = jnp.arange(length, dtype=jnp.int32)
    hann = 0.5 - 0.5 * jnp.cos(times.astype(jnp.float32) * scale)
    factor = hann[:, None] / math.sqrt(3.0 * length / 8.0)
    return jnp.concatenate([factor * cos, -factor * sin], axis=1).astype(jnp.bfloat16)


def interp_weights(offsets, frac):
    rows = []
    for shift in range(-1, 2):
        low = (offsets == shift).astype(frac.dtype)
        high = (offsets + 1 == shift).astype(frac.dtype)
        rows.append((1.0 - frac) * low + frac * high)
    return jnp.stack(rows, 0)


def shards(pressure, offsets, frac):
    cycles, sector, blocks, length = pressure.shape
    subs = offsets.shape[1]
    sub_len = length // subs
    n_az = lax.axis_size("az")
    n_tm = lax.axis_size("tm")
    forward = [(i, (i + 1) % n_az) for i in range(n_az)]
    backward = [((i + 1) % n_az, i) for i in range(n_az)]
    table = dft_table(length, FREQS)
    all_weights = jnp.repeat(interp_weights(offsets, frac), sub_len, axis=2)[:, None, None]
    fl = FREQS // n_tm
    local_rows = sector * cycles
    nb = blocks // BLOCK_CHUNKS
    result = None
    for j in range(BLOCK_CHUNKS):
        block = pressure[:, :, j * nb : (j + 1) * nb]
        weights = all_weights[:, :, :, j * nb : (j + 1) * nb]

        def transform(rows):
            return lax.dot_general(
                table, rows.reshape(-1, length), (((0,), (1,)), ((), ())),
                preferred_element_type=jnp.float32,
            )

        def split(v):
            hi = v.astype(jnp.bfloat16)
            return hi, (v - hi.astype(jnp.float32)).astype(jnp.bfloat16)

        def edge(v):
            hi, lo = split(v)
            both = transform(jnp.concatenate([hi, lo], 0))
            return both[:, : both.shape[1] // 2] + both[:, both.shape[1] // 2 :]

        to_next = edge(weights[0] * block[:, sector - 1 :].astype(jnp.float32))
        to_prev = edge(weights[2] * block[:, :1].astype(jnp.float32))
        from_prev = lax.ppermute(to_next, "az", forward)
        from_next = lax.ppermute(to_prev, "az", backward)
        zero = jnp.zeros_like(block[:, :1])
        prev = jnp.concatenate([zero, block[:, :-1]], axis=1).astype(jnp.float32)
        nxt = jnp.concatenate([block[:, 1:], zero], axis=1).astype(jnp.float32)
        total = weights[0] * prev + weights[1] * block.astype(jnp.float32) + weights[2] * nxt
        total = total.transpose(1, 0, 2, 3)
        hi = total.astype(jnp.bfloat16)
        first = split(total[:1])[1]
        last = split(total[-1:])[1]
        inner, low_first, low_last = lax.optimization_barrier(
            (transform(hi), transform(first), transform(last))
        )
        run = cycles * nb
        spectra = jnp.concatenate(
            [inner[:, :run] + low_first + from_prev, inner[:, run:-run], inner[:, -run:] + low_last + from_next],
            axis=1,
        ).astype(jnp.bfloat16)
        spectra = spectra.reshape(2, n_tm, fl, cycles * sector * nb).transpose(1, 0, 2, 3)
        shared = lax.all_to_all(spectra, "tm", 0, 0, tiled=True)
        x = shared.reshape(n_tm, 2, fl, local_rows, nb).transpose(2, 3, 0, 1, 4)
        x = x.reshape(fl, local_rows, n_tm, 2, nb)
        rows = x.reshape(fl, local_rows, n_tm * 2 * nb)
        turned = jnp.stack([x[:, :, :, 1], -x[:, :, :, 0]], 3).reshape(rows.shape)
        lhs = jnp.stack([rows, turned], 1)
        columns = lax.all_gather(rows, "az", axis=1, tiled=True)
        part = jnp.einsum("fcqk,fpk->fcqp", lhs, columns, preferred_element_type=jnp.float32)
        result = part if result is None else result + part
    return result * (1.0 / (n_tm * blocks))


def solution(mesh):
    return jax.shard_map(
        shards,
        mesh=mesh,
        in_specs=(P(None, "az", "tm", None), P("tm", None), P("tm", None)),
        out_specs=P("tm", None, "az", None),
        check_vma=False,
    )
```

```python
import math

import jax
import jax.numpy as jnp
from jax import lax
from jax.sharding import PartitionSpec as P

FREQS = 256
BLOCK_CHUNKS = 1


def dft_table(length, freqs):
    step = 64
    bins = jnp.arange(1, freqs + 1, dtype=jnp.int32)
    high = jnp.arange(length // step, dtype=jnp.int32)
    low = jnp.arange(step, dtype=jnp.int32)
    scale = 2.0 * math.pi / length
    a = (high[:, None] * step * bins[None, :] % length).astype(jnp.float32) * scale
    b = (low[:, None] * bins[None, :] % length).astype(jnp.float32) * scale
    ca, sa = jnp.cos(a)[:, None], jnp.sin(a)[:, None]
    cb, sb = jnp.cos(b)[None], jnp.sin(b)[None]
    ca, sa, cb, sb = lax.optimization_barrier((ca, sa, cb, sb))
    cos = (ca * cb - sa * sb).reshape(length, freqs)
    sin = (sa * cb + ca * sb).reshape(length, freqs)
    times = jnp.arange(length, dtype=jnp.int32)
    hann = 0.5 - 0.5 * jnp.cos(times.astype(jnp.float32) * scale)
    factor = hann[:, None] / math.sqrt(3.0 * length / 8.0)
    return jnp.concatenate([factor * cos, -factor * sin], axis=1).astype(jnp.bfloat16)


def interp_weights(offsets, frac):
    rows = []
    for shift in range(-1, 2):
        low = (offsets == shift).astype(frac.dtype)
        high = (offsets + 1 == shift).astype(frac.dtype)
        rows.append((1.0 - frac) * low + frac * high)
    return jnp.stack(rows, 0)


def shards(pressure, offsets, frac):
    cycles, sector, blocks, length = pressure.shape
    subs = offsets.shape[1]
    sub_len = length // subs
    n_az = lax.axis_size("az")
    n_tm = lax.axis_size("tm")
    forward = [(i, (i + 1) % n_az) for i in range(n_az)]
    backward = [((i + 1) % n_az, i) for i in range(n_az)]
    table = dft_table(length, FREQS)
    all_weights = jnp.repeat(interp_weights(offsets, frac), sub_len, axis=2)[:, None, None]
    fl = FREQS // n_tm
    local_rows = sector * cycles
    nb = blocks // BLOCK_CHUNKS
    result = None
    for j in range(BLOCK_CHUNKS):
        block = pressure[:, :, j * nb : (j + 1) * nb]
        left = lax.ppermute(block[:, sector - 1 :], "az", forward)
        right = lax.ppermute(block[:, :1], "az", backward)
        weights = all_weights[:, :, :, j * nb : (j + 1) * nb]
        prev = jnp.concatenate([left, block[:, :-1]], axis=1).astype(jnp.float32)
        nxt = jnp.concatenate([block[:, 1:], right], axis=1).astype(jnp.float32)
        total = weights[0] * prev + weights[1] * block.astype(jnp.float32) + weights[2] * nxt
        virtual = total.astype(jnp.bfloat16).transpose(1, 0, 2, 3).reshape(cycles * sector * nb, length)
        spectra = lax.dot_general(
            table, virtual, (((0,), (1,)), ((), ())), preferred_element_type=jnp.float32
        ).astype(jnp.bfloat16)
        spectra = spectra.reshape(2, n_tm, fl, cycles * sector * nb).transpose(1, 0, 2, 3)
        shared = lax.all_to_all(spectra, "tm", 0, 0, tiled=True)
        x = shared.reshape(n_tm, 2, fl, local_rows, nb).transpose(2, 3, 0, 1, 4)
        x = x.reshape(fl, local_rows, n_tm, 2, nb)
        rows = x.reshape(fl, local_rows, n_tm * 2 * nb)
        turned = jnp.stack([x[:, :, :, 1], -x[:, :, :, 0]], 3).reshape(rows.shape)
        lhs = jnp.stack([rows, turned], 1)
        columns = lax.all_gather(rows, "az", axis=1, tiled=True)
        part = jnp.einsum("fcqk,fpk->fcqp", lhs, columns, preferred_element_type=jnp.float32)
        result = part if result is None else result + part
    return result * (1.0 / (n_tm * blocks))


def solution(mesh):
    return jax.shard_map(
        shards,
        mesh=mesh,
        in_specs=(P(None, "az", "tm", None), P("tm", None), P("tm", None)),
        out_specs=P("tm", None, "az", None),
        check_vma=False,
    )
```

```python
import math

import jax
import jax.numpy as jnp
from jax import lax
from jax.sharding import PartitionSpec as P

FREQS = 256
BLOCK_CHUNKS = 1


def dft_table(length, freqs):
    step = 64
    bins = jnp.arange(1, freqs + 1, dtype=jnp.int32)
    high = jnp.arange(length // step, dtype=jnp.int32)
    low = jnp.arange(step, dtype=jnp.int32)
    scale = 2.0 * math.pi / length
    a = (high[:, None] * step * bins[None, :] % length).astype(jnp.float32) * scale
    b = (low[:, None] * bins[None, :] % length).astype(jnp.float32) * scale
    ca, sa = jnp.cos(a)[:, None], jnp.sin(a)[:, None]
    cb, sb = jnp.cos(b)[None], jnp.sin(b)[None]
    ca, sa, cb, sb = lax.optimization_barrier((ca, sa, cb, sb))
    cos = (ca * cb - sa * sb).reshape(length, freqs)
    sin = (sa * cb + ca * sb).reshape(length, freqs)
    times = jnp.arange(length, dtype=jnp.int32)
    hann = 0.5 - 0.5 * jnp.cos(times.astype(jnp.float32) * scale)
    factor = hann[:, None] / math.sqrt(3.0 * length / 8.0)
    return jnp.concatenate([factor * cos, -factor * sin], axis=1).astype(jnp.bfloat16)


def interp_weights(offsets, frac):
    rows = []
    for shift in range(-1, 2):
        low = (offsets == shift).astype(frac.dtype)
        high = (offsets + 1 == shift).astype(frac.dtype)
        rows.append((1.0 - frac) * low + frac * high)
    return jnp.stack(rows, 0)


def shards(pressure, offsets, frac):
    cycles, sector, blocks, length = pressure.shape
    subs = offsets.shape[1]
    sub_len = length // subs
    n_az = lax.axis_size("az")
    n_tm = lax.axis_size("tm")
    forward = [(i, (i + 1) % n_az) for i in range(n_az)]
    backward = [((i + 1) % n_az, i) for i in range(n_az)]
    table = dft_table(length, FREQS)
    all_weights = jnp.repeat(interp_weights(offsets, frac), sub_len, axis=2)[:, None, None]
    fl = FREQS // n_tm
    local_rows = sector * cycles
    nb = blocks // BLOCK_CHUNKS
    result = None
    for j in range(BLOCK_CHUNKS):
        block = pressure[:, :, j * nb : (j + 1) * nb]
        left = lax.ppermute(block[:, sector - 1 :], "az", forward)
        right = lax.ppermute(block[:, :1], "az", backward)
        weights = all_weights[:, :, :, j * nb : (j + 1) * nb]

        def transform(total):
            rows = total.astype(jnp.bfloat16).transpose(1, 0, 2, 3).reshape(-1, length)
            return lax.dot_general(
                table, rows, (((0,), (1,)), ((), ())), preferred_element_type=jnp.float32
            )

        def virtual(prev, mid, nxt):
            return (
                weights[0] * prev.astype(jnp.float32)
                + weights[1] * mid.astype(jnp.float32)
                + weights[2] * nxt.astype(jnp.float32)
            )

        inner = transform(virtual(block[:, :-2], block[:, 1:-1], block[:, 2:]))
        first = transform(virtual(left, block[:, :1], block[:, 1:2]))
        last = transform(virtual(block[:, -2:-1], block[:, -1:], right))
        spectra = jnp.concatenate([first, inner, last], axis=1).astype(jnp.bfloat16)
        spectra = spectra.reshape(2, n_tm, fl, cycles * sector * nb).transpose(1, 0, 2, 3)
        shared = lax.all_to_all(spectra, "tm", 0, 0, tiled=True)
        x = shared.reshape(n_tm, 2, fl, local_rows, nb).transpose(2, 3, 0, 1, 4)
        x = x.reshape(fl, local_rows, n_tm, 2, nb)
        rows = x.reshape(fl, local_rows, n_tm * 2 * nb)
        turned = jnp.stack([x[:, :, :, 1], -x[:, :, :, 0]], 3).reshape(rows.shape)
        lhs = jnp.stack([rows, turned], 1)
        columns = lax.all_gather(rows, "az", axis=1, tiled=True)
        part = jnp.einsum("fcqk,fpk->fcqp", lhs, columns, preferred_element_type=jnp.float32)
        result = part if result is None else result + part
    return result * (1.0 / (n_tm * blocks))


def solution(mesh):
    return jax.shard_map(
        shards,
        mesh=mesh,
        in_specs=(P(None, "az", "tm", None), P("tm", None), P("tm", None)),
        out_specs=P("tm", None, "az", None),
        check_vma=False,
    )
```
